128 devices in a mesh: row: 8 (over z_lo, y), col: 16 (over x, z_hi, core).
Axes of the slice: x: 4, y: 4, z: 4 (z_hi: 2, z_lo: 2; z = z_hi * 2 + z_lo), core: 2. Of those that a mesh axis runs over, the one named last changes fastest.
Arguments:
- factors: bfloat16 [10240, 3, 2048], P(('row', 'col')), may hold values from -0.59765625 to 0.59765625
- occ_energy: float32 [300], replicated, may hold values from -3 to -0.5
- vir_energy: float32 [2048], replicated, may hold values from 0.3 to 4
- slab_orbitals: int32 [3], replicated, may hold values from 0 to 299
- pair_list: int32 [16, 2], replicated, may hold values from 0 to 2
- pair_state: int32 [16], replicated, may hold values from 0 to 3
- state_shift: float32 [4], replicated, may hold values from 0.1 to 1
Outputs:
- amplitudes: float32 [16, 2048, 2048], P(None, 'row', 'col')
The draws below stay inside these ranges and needn't reach their ends.
All inputs are finite; a program needn't handle non-finite values.
Results may differ from the reference program's by a relative error of at most 0.0003.
Values may be sent and summed in bfloat16 or wider, within the bound.
No kernel may reach another device: no remote copies, remote signals or barrier semaphores. Data moves between devices by JAX's collectives and lax.ppermute only.
A program may use at most 192 MiB of HBM per device.

```python
import math
import jax
import jax.numpy as jnp
from jax import lax

NAUX = 10240
NV = 2048
NCORE = 300
NOCC = 3
NPAIR = 16
NSTATE = 4


def place_ends(entries, key, low, top_value):
    index_at = [jax.random.randint(jax.random.fold_in(key, axis), (), 0, length) for axis, length in enumerate(entries.shape)]
    main_axis = entries.shape.index(max(entries.shape))
    beside = index_at[:main_axis] + [(index_at[main_axis] + 1) % entries.shape[main_axis]] + index_at[main_axis + 1:]
    return entries.at[tuple(index_at)].set(low).at[tuple(beside)].set(top_value)


def block_levels(key, shape, split, smallest, top_value):
    def one(axis_at, shards_of):
        heights = jax.random.uniform(jax.random.fold_in(jax.random.fold_in(key, 6), axis_at), (shards_of,), jnp.float32, smallest / len(split), top_value / len(split))
        return jnp.repeat(jnp.exp(heights), shape[axis_at] // shards_of).reshape((-1,) + (1,) * (len(shape) - axis_at - 1))

    loudness = one(*split[0])
    for cut in split[1:]:
        loudness = loudness * one(*cut)
    return loudness


def normal_values(rng, dims, width, reach, pieces=(), dtype=jnp.bfloat16):
    loudness = block_levels(rng, dims, pieces, -0.22, 0.18) if pieces else 1.0
    drawn = jax.random.normal(rng, dims, jnp.float32) * width * loudness
    return jnp.minimum(jnp.maximum(drawn, -reach), reach).astype(dtype)


def setup_inputs(seed: int = 0) -> dict:
    splits = jax.random.split(jax.random.key(seed), 8)
    return {
        "factors": normal_values(splits[0], (NAUX, NOCC, NV), 0.1, 0.59765625, ((0, 128),)),
        "occ_energy": jnp.clip(jax.random.uniform(splits[1], (NCORE,), jnp.float32, -3.0, -0.5), -3.0, -0.5),
        "vir_energy": jnp.clip(jax.random.uniform(splits[2], (NV,), jnp.float32, 0.3, 4.0), 0.3, 4.0),
        "slab_orbitals": jax.random.randint(splits[3], (NOCC,), 0, NCORE).astype(jnp.int32),
        "pair_list": place_ends(jax.random.randint(splits[4], (NPAIR, 2), 0, NOCC), jax.random.fold_in(splits[4], 1), 0, NOCC - 1).astype(jnp.int32),
        "pair_state": place_ends(jax.random.randint(splits[5], (NPAIR,), 0, NSTATE), jax.random.fold_in(splits[5], 1), 0, NSTATE - 1).astype(jnp.int32),
        "state_shift": jnp.clip(jnp.exp(jax.random.uniform(splits[6], (NSTATE,), jnp.float32, math.log(0.1), math.log(1.0))), 0.1, 1.0),
    }


def reference(factors, occ_energy, vir_energy, slab_orbitals, pair_list, pair_state, state_shift):
    blocks = []
    for pair in range(NPAIR):
        first = pair_list[pair, 0]
        second = pair_list[pair, 1]
        left = lax.dynamic_index_in_dim(factors, first, 1, keepdims=False)
        right = lax.dynamic_index_in_dim(factors, second, 1, keepdims=False)
        kernel = lax.dot_general(left, right, (((0,), (0,)), ((), ())), preferred_element_type=jnp.float32)
        e_first = occ_energy[slab_orbitals[first]]
        e_second = occ_energy[slab_orbitals[second]]
        denom = (vir_energy[:, None] + vir_energy[None, :]) - e_first - e_second + state_shift[pair_state[pair]]
        blocks.append(-kernel / denom)
    return jnp.stack(blocks)
```

```python
import jax
import jax.numpy as jnp
from jax import lax
from jax.sharding import PartitionSpec as P


def shards(factors, occ_energy, vir_energy, slab_orbitals, pair_list, pair_state, state_shift):
    n_row = lax.axis_size("row")
    n_col = lax.axis_size("col")
    local_aux, nocc, nvir = factors.shape
    rows_a = nvir // n_row
    cols_b = nvir // n_col
    spread_a = lax.all_to_all(
        factors.reshape(local_aux, nocc, n_row, rows_a), "row", split_axis=2, concat_axis=0, tiled=True
    ).reshape(n_row * local_aux, nocc, rows_a)
    block_a = lax.all_gather(spread_a, "col", axis=0, tiled=True)
    spread_b = lax.all_to_all(
        factors.reshape(local_aux, nocc, n_col, cols_b), "col", split_axis=2, concat_axis=0, tiled=True
    ).reshape(n_col * local_aux, nocc, cols_b)
    block_b = lax.all_gather(spread_b, "row", axis=0, tiled=True)
    block_a = block_a.reshape(n_col, n_row, local_aux, nocc, rows_a)
    block_b = block_b.reshape(n_row, n_col, local_aux, nocc, cols_b)
    gram = jnp.einsum(
        "crpia,rcpjb->ijab", block_a, block_b, preferred_element_type=jnp.float32
    ).reshape(nocc * nocc, rows_a, cols_b)
    first = pair_list[:, 0]
    second = pair_list[:, 1]
    kernel = jnp.take(gram, first * nocc + second, axis=0)
    vir_a = lax.dynamic_slice_in_dim(vir_energy, lax.axis_index("row") * rows_a, rows_a)
    vir_b = lax.dynamic_slice_in_dim(vir_energy, lax.axis_index("col") * cols_b, cols_b)
    e_first = occ_energy[slab_orbitals[first]]
    e_second = occ_energy[slab_orbitals[second]]
    shift = state_shift[pair_state]
    denom = (
        (vir_a[None, :, None] + vir_b[None, None, :])
        - e_first[:, None, None]
        - e_second[:, None, None]
        + shift[:, None, None]
    )
    return -kernel / denom


def solution(mesh):
    placed = (P(("row", "col"), None, None), P(), P(), P(), P(), P(), P())
    return jax.shard_map(
        shards, mesh=mesh, in_specs=placed, out_specs=P(None, "row", "col"), check_vma=False
    )
```

```python
import jax
import jax.numpy as jnp
from jax import lax
from jax.sharding import PartitionSpec as P


def row_ring(n_row):
    half = n_row // 2
    return list(range(half)) + [half + y for y in reversed(range(half))]


def ring_gather(shard, axis, ring):
    n = len(ring)
    position = [0] * n
    for k, r in enumerate(ring):
        position[r] = k
    right = [(ring[k], ring[(k + 1) % n]) for k in range(n)]
    left = [(ring[k], ring[(k - 1) % n]) for k in range(n)]
    ring_arr = jnp.array(ring, dtype=jnp.int32)
    me = lax.axis_index(axis)
    my_pos = jnp.array(position, dtype=jnp.int32)[me]
    out = jnp.zeros((n,) + shard.shape, shard.dtype)
    out = lax.dynamic_update_index_in_dim(out, shard, me, 0)
    go_right = go_left = shard
    n_right = n // 2
    n_left = n - 1 - n_right
    for step in range(1, n_right + 1):
        go_right = lax.ppermute(go_right, axis, right)
        out = lax.dynamic_update_index_in_dim(out, go_right, ring_arr[(my_pos - step) % n], 0)
        if step <= n_left:
            go_left = lax.ppermute(go_left, axis, left)
            out = lax.dynamic_update_index_in_dim(out, go_left, ring_arr[(my_pos + step) % n], 0)
    return out


def shards(factors, occ_energy, vir_energy, slab_orbitals, pair_list, pair_state, state_shift):
    n_row = lax.axis_size("row")
    n_col = lax.axis_size("col")
    local_aux, nocc, nvir = factors.shape
    rows_a = nvir // n_row
    cols_b = nvir // n_col
    spread_a = lax.all_to_all(
        factors.reshape(local_aux, nocc, n_row, rows_a), "row", split_axis=2, concat_axis=0, tiled=True
    ).reshape(n_row * local_aux, nocc, rows_a)
    block_a = lax.all_gather(spread_a, "col", axis=0, tiled=True)
    spread_b = lax.all_to_all(
        factors.reshape(local_aux, nocc, n_col, cols_b), "col", split_axis=2, concat_axis=0, tiled=True
    ).reshape(n_col * local_aux, nocc, cols_b)
    block_b = ring_gather(spread_b, "row", row_ring(n_row))
    block_a = block_a.reshape(n_col, n_row, local_aux, nocc, rows_a)
    block_b = block_b.reshape(n_row, n_col, local_aux, nocc, cols_b)
    gram = jnp.einsum(
        "crpia,rcpjb->ijab", block_a, block_b, preferred_element_type=jnp.float32
    ).reshape(nocc * nocc, rows_a, cols_b)
    first = pair_list[:, 0]
    second = pair_list[:, 1]
    kernel = jnp.take(gram, first * nocc + second, axis=0)
    vir_a = lax.dynamic_slice_in_dim(vir_energy, lax.axis_index("row") * rows_a, rows_a)
    vir_b = lax.dynamic_slice_in_dim(vir_energy, lax.axis_index("col") * cols_b, cols_b)
    e_first = occ_energy[slab_orbitals[first]]
    e_second = occ_energy[slab_orbitals[second]]
    shift = state_shift[pair_state]
    denom = (
        (vir_a[None, :, None] + vir_b[None, None, :])
        - e_first[:, None, None]
        - e_second[:, None, None]
        + shift[:, None, None]
    )
    return -kernel / denom


def solution(mesh):
    placed = (P(("row", "col"), None, None), P(), P(), P(), P(), P(), P())
    return jax.shard_map(
        shards, mesh=mesh, in_specs=placed, out_specs=P(None, "row", "col"), check_vma=False
    )
```

```python
import jax
import jax.numpy as jnp
from jax import lax
from jax.sharding import Mesh, PartitionSpec as P


def row_ring(n_row):
    half = n_row // 2
    return list(range(half)) + [half + y for y in reversed(range(half))]


def ring_gather(shard, axis, ring):
    n = len(ring)
    position = [0] * n
    for k, r in enumerate(ring):
        position[r] = k
    right = [(ring[k], ring[(k + 1) % n]) for k in range(n)]
    left = [(ring[k], ring[(k - 1) % n]) for k in range(n)]
    ring_arr = jnp.array(ring, dtype=jnp.int32)
    me = lax.axis_index(axis)
    my_pos = jnp.array(position, dtype=jnp.int32)[me]
    out = jnp.zeros((n,) + shard.shape, shard.dtype)
    out = lax.dynamic_update_index_in_dim(out, shard, me, 0)
    go_right = go_left = shard
    n_right = n // 2
    n_left = n - 1 - n_right
    for step in range(1, n_right + 1):
        go_right = lax.ppermute(go_right, axis, right)
        out = lax.dynamic_update_index_in_dim(out, go_right, ring_arr[(my_pos - step) % n], 0)
        if step <= n_left:
            go_left = lax.ppermute(go_left, axis, left)
            out = lax.dynamic_update_index_in_dim(out, go_left, ring_arr[(my_pos + step) % n], 0)
    return out


def shards(factors, occ_energy, vir_energy, slab_orbitals, pair_list, pair_state, state_shift):
    n_row = lax.axis_size("row")
    n_colx = lax.axis_size("colx")
    n_core = lax.axis_size("core")
    n_col = n_colx * n_core
    local_aux, nocc, nvir = factors.shape
    rows_a = nvir // n_row
    cols_b = nvir // n_col
    spread_a = lax.all_to_all(
        factors.reshape(local_aux, nocc, n_row, rows_a), "row", split_axis=2, concat_axis=0, tiled=True
    ).reshape(n_row * local_aux, nocc, rows_a)
    half_a = lax.all_gather(spread_a, "colx", axis=0, tiled=True)
    other_a = lax.ppermute(half_a, "core", [(k, (k + 1) % n_core) for k in range(n_core)])
    spread_b = lax.all_to_all(
        factors.reshape(local_aux, nocc, n_col, cols_b), ("colx", "core"), split_axis=2, concat_axis=0, tiled=True
    ).reshape(n_col * local_aux, nocc, cols_b)
    block_b = ring_gather(spread_b, "row", row_ring(n_row))
    block_b = block_b.reshape(n_row, n_colx, n_core, local_aux, nocc, cols_b)
    me_core = lax.axis_index("core")
    contract = "xrpia,rxpjb->ijab"
    gram = jnp.einsum(
        contract,
        half_a.reshape(n_colx, n_row, local_aux, nocc, rows_a),
        lax.dynamic_index_in_dim(block_b, me_core, 2, keepdims=False),
        preferred_element_type=jnp.float32,
    ) + jnp.einsum(
        contract,
        other_a.reshape(n_colx, n_row, local_aux, nocc, rows_a),
        lax.dynamic_index_in_dim(block_b, (me_core + n_core - 1) % n_core, 2, keepdims=False),
        preferred_element_type=jnp.float32,
    )
    gram = gram.reshape(nocc * nocc, rows_a, cols_b)
    first = pair_list[:, 0]
    second = pair_list[:, 1]
    kernel = jnp.take(gram, first * nocc + second, axis=0)
    vir_a = lax.dynamic_slice_in_dim(vir_energy, lax.axis_index("row") * rows_a, rows_a)
    col_index = lax.axis_index("colx") * n_core + me_core
    vir_b = lax.dynamic_slice_in_dim(vir_energy, col_index * cols_b, cols_b)
    e_first = occ_energy[slab_orbitals[first]]
    e_second = occ_energy[slab_orbitals[second]]
    shift = state_shift[pair_state]
    denom = (
        (vir_a[None, :, None] + vir_b[None, None, :])
        - e_first[:, None, None]
        - e_second[:, None, None]
        + shift[:, None, None]
    )
    return -kernel / denom


def solution(mesh):
    n_row, n_col = mesh.devices.shape
    sub = Mesh(mesh.devices.reshape(n_row, n_col // 2, 2), ("row", "colx", "core"))
    placed = (P(("row", "colx", "core"), None, None), P(), P(), P(), P(), P(), P())
    return jax.shard_map(
        shards, mesh=sub, in_specs=placed, out_specs=P(None, "row", ("colx", "core")), check_vma=False
    )
```

```python
import jax
import jax.numpy as jnp
from jax import lax
from jax.sharding import Mesh, PartitionSpec as P


def y_ring_gather(shard, axis):
    n = lax.axis_size(axis)
    me = lax.axis_index(axis)
    right = [(k, (k + 1) % n) for k in range(n)]
    left = [(k, (k - 1) % n) for k in range(n)]
    out = jnp.zeros((n,) + shard.shape, shard.dtype)
    out = lax.dynamic_update_index_in_dim(out, shard, me, 0)
    go_right = go_left = shard
    steps = n // 2
    for step in range(1, steps + 1):
        if step < steps or n % 2 == 1:
            go_right = lax.ppermute(go_right, axis, right)
            go_left = lax.ppermute(go_left, axis, left)
            out = lax.dynamic_update_index_in_dim(out, go_right, (me - step) % n, 0)
            out = lax.dynamic_update_index_in_dim(out, go_left, (me + step) % n, 0)
        else:
            half = shard.shape[0] // 2
            from_left = lax.ppermute(go_right[:half], axis, right)
            from_right = lax.ppermute(go_left[half:], axis, left)
            far = jnp.concatenate([from_left, from_right], axis=0)
            out = lax.dynamic_update_index_in_dim(out, far, (me - step) % n, 0)
    return out


def shards(factors, occ_energy, vir_energy, slab_orbitals, pair_list, pair_state, state_shift):
    n_zl = lax.axis_size("zl")
    n_y = lax.axis_size("y")
    n_row = n_zl * n_y
    n_col = lax.axis_size("col")
    local_aux, nocc, nvir = factors.shape
    rows_a = nvir // n_row
    cols_b = nvir // n_col
    me_zl = lax.axis_index("zl")
    row_index = me_zl * n_y + lax.axis_index("y")
    spread_a = lax.all_to_all(
        factors.reshape(local_aux, nocc, n_row, rows_a), ("zl", "y"), split_axis=2, concat_axis=0, tiled=True
    ).reshape(n_row * local_aux, nocc, rows_a)
    block_a = lax.all_gather(spread_a, "col", axis=0, tiled=True)
    partner = lax.ppermute(factors, "zl", [(k, (k + 1) % n_zl) for k in range(n_zl)])
    pair = jnp.where(me_zl == 0, jnp.stack([factors, partner]), jnp.stack([partner, factors]))
    spread_b = lax.all_to_all(
        pair.reshape(n_zl * local_aux, nocc, n_col, cols_b), "col", split_axis=2, concat_axis=0, tiled=True
    ).reshape(n_col * n_zl * local_aux, nocc, cols_b)
    block_b = y_ring_gather(spread_b, "y")
    block_a = block_a.reshape(n_col, n_zl, n_y, local_aux, nocc, rows_a)
    block_b = block_b.reshape(n_y, n_col, n_zl, local_aux, nocc, cols_b)
    gram = jnp.einsum(
        "czypia,yczpjb->ijab",
        block_a,
        block_b,
        preferred_element_type=jnp.float32,
    ).reshape(nocc * nocc, rows_a, cols_b)
    first = pair_list[:, 0]
    second = pair_list[:, 1]
    kernel = jnp.take(gram, first * nocc + second, axis=0)
    vir_a = lax.dynamic_slice_in_dim(vir_energy, row_index * rows_a, rows_a)
    vir_b = lax.dynamic_slice_in_dim(vir_energy, lax.axis_index("col") * cols_b, cols_b)
    e_first = occ_energy[slab_orbitals[first]]
    e_second = occ_energy[slab_orbitals[second]]
    shift = state_shift[pair_state]
    denom = (
        (vir_a[None, :, None] + vir_b[None, None, :])
        - e_first[:, None, None]
        - e_second[:, None, None]
        + shift[:, None, None]
    )
    return -kernel / denom


def solution(mesh):
    n_row, n_col = mesh.devices.shape
    sub = Mesh(mesh.devices.reshape(2, n_row // 2, n_col), ("zl", "y", "col"))
    placed = (P(("zl", "y", "col"), None, None), P(), P(), P(), P(), P(), P())
    return jax.shard_map(
        shards, mesh=sub, in_specs=placed, out_specs=P(None, ("zl", "y"), "col"), check_vma=False
    )
```

```python
import jax
import jax.numpy as jnp
from jax import lax
from jax.sharding import Mesh, PartitionSpec as P


def y_ring_gather(shard, axis):
    n = lax.axis_size(axis)
    me = lax.axis_index(axis)
    right = [(k, (k + 1) % n) for k in range(n)]
    left = [(k, (k - 1) % n) for k in range(n)]
    out = jnp.zeros((n,) + shard.shape, shard.dtype)
    out = lax.dynamic_update_index_in_dim(out, shard, me, 0)
    go_right = go_left = shard
    steps = n // 2
    for step in range(1, steps + 1):
        if step < steps or n % 2 == 1:
            go_right = lax.ppermute(go_right, axis, right)
            go_left = lax.ppermute(go_left, axis, left)
            out = lax.dynamic_update_index_in_dim(out, go_right, (me - step) % n, 0)
            out = lax.dynamic_update_index_in_dim(out, go_left, (me + step) % n, 0)
        else:
            half = shard.shape[0] // 2
            from_left = lax.ppermute(go_right[:half], axis, right)
            from_right = lax.ppermute(go_left[half:], axis, left)
            far = jnp.concatenate([from_left, from_right], axis=0)
            out = lax.dynamic_update_index_in_dim(out, far, (me - step) % n, 0)
    return out


def swap_pair(part, axis):
    n = lax.axis_size(axis)
    other = lax.ppermute(part, axis, [(k, (k + 1) % n) for k in range(n)])
    return jnp.where(lax.axis_index(axis) == 0, jnp.stack([part, other]), jnp.stack([other, part]))


def shards(factors, occ_energy, vir_energy, slab_orbitals, pair_list, pair_state, state_shift):
    n_zl = lax.axis_size("zl")
    n_y = lax.axis_size("y")
    n_x = lax.axis_size("x")
    n_zh = lax.axis_size("zh")
    n_core = lax.axis_size("core")
    n_row = n_zl * n_y
    n_col = n_x * n_zh * n_core
    local_aux, nocc, nvir = factors.shape
    rows_a = nvir // n_row
    cols_b = nvir // n_col
    row_index = lax.axis_index("zl") * n_y + lax.axis_index("y")
    col_index = (lax.axis_index("x") * n_zh + lax.axis_index("zh")) * n_core + lax.axis_index("core")
    spread_a = lax.all_to_all(
        factors.reshape(local_aux, nocc, n_row, rows_a), ("zl", "y"), split_axis=2, concat_axis=0, tiled=True
    )
    pair_a = swap_pair(spread_a.reshape(n_row * local_aux, nocc, rows_a), "zh")
    block_a = lax.all_gather(pair_a, ("x", "core"), axis=0, tiled=True)
    spread_b = lax.all_to_all(
        factors.reshape(local_aux, nocc, n_col, cols_b), ("x", "zh", "core"), split_axis=2, concat_axis=0, tiled=True
    )
    pair_b = swap_pair(spread_b.reshape(n_col * local_aux, nocc, cols_b), "zl")
    block_b = y_ring_gather(pair_b.reshape(n_zl * n_col * local_aux, nocc, cols_b), "y")
    block_a = block_a.reshape(n_x, n_core, n_zh, n_zl, n_y, local_aux, nocc, rows_a)
    block_b = block_b.reshape(n_y, n_zl, n_x, n_zh, n_core, local_aux, nocc, cols_b)
    gram = jnp.einsum(
        "xchzypia,yzxhcpjb->ijab",
        block_a,
        block_b,
        preferred_element_type=jnp.float32,
    ).reshape(nocc * nocc, rows_a, cols_b)
    first = pair_list[:, 0]
    second = pair_list[:, 1]
    kernel = jnp.take(gram, first * nocc + second, axis=0)
    vir_a = lax.dynamic_slice_in_dim(vir_energy, row_index * rows_a, rows_a)
    vir_b = lax.dynamic_slice_in_dim(vir_energy, col_index * cols_b, cols_b)
    e_first = occ_energy[slab_orbitals[first]]
    e_second = occ_energy[slab_orbitals[second]]
    shift = state_shift[pair_state]
    denom = (
        (vir_a[None, :, None] + vir_b[None, None, :])
        - e_first[:, None, None]
        - e_second[:, None, None]
        + shift[:, None, None]
    )
    return -kernel / denom


def solution(mesh):
    n_row, n_col = mesh.devices.shape
    sub = Mesh(mesh.devices.reshape(2, n_row // 2, n_col // 4, 2, 2), ("zl", "y", "x", "zh", "core"))
    placed = (P(("zl", "y", "x", "zh", "core"), None, None), P(), P(), P(), P(), P(), P())
    return jax.shard_map(
        shards, mesh=sub, in_specs=placed, out_specs=P(None, ("zl", "y"), ("x", "zh", "core")), check_vma=False
    )
```

```python
import jax
import jax.numpy as jnp
from jax import lax
from jax.sharding import Mesh, PartitionSpec as P


def y_ring_gather(shard, axis):
    n = lax.axis_size(axis)
    me = lax.axis_index(axis)
    right = [(k, (k + 1) % n) for k in range(n)]
    left = [(k, (k - 1) % n) for k in range(n)]
    out = jnp.zeros((n,) + shard.shape, shard.dtype)
    out = lax.dynamic_update_index_in_dim(out, shard, me, 0)
    go_right = go_left = shard
    steps = n // 2
    for step in range(1, steps + 1):
        if step < steps or n % 2 == 1:
            go_right = lax.ppermute(go_right, axis, right)
            go_left = lax.ppermute(go_left, axis, left)
            out = lax.dynamic_update_index_in_dim(out, go_right, (me - step) % n, 0)
            out = lax.dynamic_update_index_in_dim(out, go_left, (me + step) % n, 0)
        else:
            half = shard.shape[0] // 2
            from_left = lax.ppermute(go_right[:half], axis, right)
            from_right = lax.ppermute(go_left[half:], axis, left)
            far = jnp.concatenate([from_left, from_right], axis=0)
            out = lax.dynamic_update_index_in_dim(out, far, (me - step) % n, 0)
    return out


def swap_pair(part, axis):
    n = lax.axis_size(axis)
    other = lax.ppermute(part, axis, [(k, (k + 1) % n) for k in range(n)])
    return jnp.where(lax.axis_index(axis) == 0, jnp.stack([part, other]), jnp.stack([other, part]))


def shards(factors, occ_energy, vir_energy, slab_orbitals, pair_list, pair_state, state_shift):
    n_zl = lax.axis_size("zl")
    n_y = lax.axis_size("y")
    n_x = lax.axis_size("x")
    n_zh = lax.axis_size("zh")
    n_core = lax.axis_size("core")
    n_row = n_zl * n_y
    n_col = n_x * n_zh * n_core
    local_aux, nocc, nvir = factors.shape
    rows_a = nvir // n_row
    cols_b = nvir // n_col
    row_index = lax.axis_index("zl") * n_y + lax.axis_index("y")
    col_index = (lax.axis_index("x") * n_zh + lax.axis_index("zh")) * n_core + lax.axis_index("core")
    spread_a = lax.all_to_all(
        factors.reshape(local_aux, nocc, n_row, rows_a), ("zl", "y"), split_axis=2, concat_axis=0, tiled=True
    )
    spread_a = spread_a.reshape(n_row * local_aux, nocc, rows_a)
    other_a = lax.ppermute(spread_a, "zh", [(k, (k + 1) % n_zh) for k in range(n_zh)])
    spread_b = lax.all_to_all(
        factors.reshape(local_aux, nocc, n_col, cols_b), ("x", "zh", "core"), split_axis=2, concat_axis=0, tiled=True
    )
    other_a, spread_b = lax.optimization_barrier((other_a, spread_b))
    first_zh = lax.axis_index("zh") == 0
    pair_a = jnp.where(first_zh, jnp.stack([spread_a, other_a]), jnp.stack([other_a, spread_a]))
    block_a = lax.all_gather(pair_a, ("x", "core"), axis=0, tiled=True)
    pair_b = swap_pair(spread_b.reshape(n_col * local_aux, nocc, cols_b), "zl")
    block_b = y_ring_gather(pair_b.reshape(n_zl * n_col * local_aux, nocc, cols_b), "y")
    block_a = block_a.reshape(n_x, n_core, n_zh, n_zl, n_y, local_aux, nocc, rows_a)
    block_b = block_b.reshape(n_y, n_zl, n_x, n_zh, n_core, local_aux, nocc, cols_b)
    gram = jnp.einsum(
        "xchzypia,yzxhcpjb->ijab",
        block_a,
        block_b,
        preferred_element_type=jnp.float32,
    ).reshape(nocc * nocc, rows_a, cols_b)
    first = pair_list[:, 0]
    second = pair_list[:, 1]
    kernel = jnp.take(gram, first * nocc + second, axis=0)
    vir_a = lax.dynamic_slice_in_dim(vir_energy, row_index * rows_a, rows_a)
    vir_b = lax.dynamic_slice_in_dim(vir_energy, col_index * cols_b, cols_b)
    e_first = occ_energy[slab_orbitals[first]]
    e_second = occ_energy[slab_orbitals[second]]
    shift = state_shift[pair_state]
    denom = (
        (vir_a[None, :, None] + vir_b[None, None, :])
        - e_first[:, None, None]
        - e_second[:, None, None]
        + shift[:, None, None]
    )
    return -kernel / denom


def solution(mesh):
    n_row, n_col = mesh.devices.shape
    sub = Mesh(mesh.devices.reshape(2, n_row // 2, n_col // 4, 2, 2), ("zl", "y", "x", "zh", "core"))
    placed = (P(("zl", "y", "x", "zh", "core"), None, None), P(), P(), P(), P(), P(), P())
    return jax.shard_map(
        shards, mesh=sub, in_specs=placed, out_specs=P(None, ("zl", "y"), ("x", "zh", "core")), check_vma=False
    )
```

```python
import jax
import jax.numpy as jnp
from jax import lax
from jax.sharding import Mesh, PartitionSpec as P


def ring_into(out, lead, shard, axis):
    n = lax.axis_size(axis)
    me = lax.axis_index(axis)
    right = [(k, (k + 1) % n) for k in range(n)]
    left = [(k, (k - 1) % n) for k in range(n)]
    zeros = (0,) * shard.ndim

    def put(buf, piece, index, offset=0):
        start = (lead, index, offset) + zeros[1:]
        return lax.dynamic_update_slice(buf, piece[None, None], start)

    out = put(out, shard, me)
    go_right = go_left = shard
    steps = n // 2
    for step in range(1, steps + 1):
        if step < steps or n % 2 == 1:
            go_right = lax.ppermute(go_right, axis, right)
            go_left = lax.ppermute(go_left, axis, left)
            out = put(out, go_right, (me - step) % n)
            out = put(out, go_left, (me + step) % n)
        else:
            half = shard.shape[0] // 2
            from_left = lax.ppermute(go_right[:half], axis, right)
            from_right = lax.ppermute(go_left[half:], axis, left)
            out = put(out, from_left, (me - step) % n)
            out = put(out, from_right, (me - step) % n, half)
    return out


def shards(factors, occ_energy, vir_energy, slab_orbitals, pair_list, pair_state, state_shift):
    n_zl = lax.axis_size("zl")
    n_y = lax.axis_size("y")
    n_x = lax.axis_size("x")
    n_zh = lax.axis_size("zh")
    n_core = lax.axis_size("core")
    n_row = n_zl * n_y
    n_col = n_x * n_zh * n_core
    local_aux, nocc, nvir = factors.shape
    rows_a = nvir // n_row
    cols_b = nvir // n_col
    row_index = lax.axis_index("zl") * n_y + lax.axis_index("y")
    col_index = (lax.axis_index("x") * n_zh + lax.axis_index("zh")) * n_core + lax.axis_index("core")
    spread_a = lax.all_to_all(
        factors.reshape(local_aux, nocc, n_row, rows_a), ("zl", "y"), split_axis=2, concat_axis=0, tiled=True
    )
    spread_a = spread_a.reshape(n_row * local_aux, nocc, rows_a)
    other_a = lax.ppermute(spread_a, "zh", [(k, (k + 1) % n_zh) for k in range(n_zh)])
    spread_b = lax.all_to_all(
        factors.reshape(local_aux, nocc, n_col, cols_b), ("x", "zh", "core"), split_axis=2, concat_axis=0, tiled=True
    )
    other_a, spread_b = lax.optimization_barrier((other_a, spread_b))
    first_zh = lax.axis_index("zh") == 0
    pair_a = jnp.where(first_zh, jnp.stack([spread_a, other_a]), jnp.stack([other_a, spread_a]))
    block_a = lax.all_gather(pair_a, ("x", "core"), axis=0, tiled=True)
    spread_b = spread_b.reshape(n_col * local_aux, nocc, cols_b)
    other_b = lax.ppermute(spread_b, "zl", [(k, (k + 1) % n_zl) for k in range(n_zl)])
    me_zl = lax.axis_index("zl")
    block_b = jnp.zeros((n_zl, n_y) + spread_b.shape, spread_b.dtype)
    block_b = ring_into(block_b, me_zl, spread_b, "y")
    block_b = ring_into(block_b, (me_zl + 1) % n_zl, other_b, "y")
    block_a = block_a.reshape(n_x, n_core, n_zh, n_zl, n_y, local_aux, nocc, rows_a)
    block_b = block_b.reshape(n_zl, n_y, n_x, n_zh, n_core, local_aux, nocc, cols_b)
    gram = jnp.einsum(
        "xchzypia,zyxhcpjb->ijab",
        block_a,
        block_b,
        preferred_element_type=jnp.float32,
    ).reshape(nocc * nocc, rows_a, cols_b)
    first = pair_list[:, 0]
    second = pair_list[:, 1]
    kernel = jnp.take(gram, first * nocc + second, axis=0)
    vir_a = lax.dynamic_slice_in_dim(vir_energy, row_index * rows_a, rows_a)
    vir_b = lax.dynamic_slice_in_dim(vir_energy, col_index * cols_b, cols_b)
    e_first = occ_energy[slab_orbitals[first]]
    e_second = occ_energy[slab_orbitals[second]]
    shift = state_shift[pair_state]
    denom = (
        (vir_a[None, :, None] + vir_b[None, None, :])
        - e_first[:, None, None]
        - e_second[:, None, None]
        + shift[:, None, None]
    )
    return -kernel / denom


def solution(mesh):
    n_row, n_col = mesh.devices.shape
    sub = Mesh(mesh.devices.reshape(2, n_row // 2, n_col // 4, 2, 2), ("zl", "y", "x", "zh", "core"))
    placed = (P(("zl", "y", "x", "zh", "core"), None, None), P(), P(), P(), P(), P(), P())
    return jax.shard_map(
        shards, mesh=sub, in_specs=placed, out_specs=P(None, ("zl", "y"), ("x", "zh", "core")), check_vma=False
    )
```

```python
import jax
import jax.numpy as jnp
from jax import lax
from jax.sharding import Mesh, PartitionSpec as P


def ring_into(out, lead, shard, axis):
    n = lax.axis_size(axis)
    me = lax.axis_index(axis)
    right = [(k, (k + 1) % n) for k in range(n)]
    left = [(k, (k - 1) % n) for k in range(n)]
    zeros = (0,) * shard.ndim

    def put(buf, piece, index, offset=0):
        start = (lead, index, offset) + zeros[1:]
        return lax.dynamic_update_slice(buf, piece[None, None], start)

    out = put(out, shard, me)
    go_right = go_left = shard
    steps = n // 2
    for step in range(1, steps + 1):
        if step < steps or n % 2 == 1:
            go_right = lax.ppermute(go_right, axis, right)
            go_left = lax.ppermute(go_left, axis, left)
            out = put(out, go_right, (me - step) % n)
            out = put(out, go_left, (me + step) % n)
        else:
            half = shard.shape[0] // 2
            from_left = lax.ppermute(go_right[:half], axis, right)
            from_right = lax.ppermute(go_left[half:], axis, left)
            out = put(out, from_left, (me - step) % n)
            out = put(out, from_right, (me - step) % n, half)
    return out


def permute_exchange(blocks, axes, me, n):
    pieces = [lax.dynamic_index_in_dim(blocks, me, 2, keepdims=False)]
    for shift in range(1, n):
        send = lax.dynamic_index_in_dim(blocks, (me + shift) % n, 2, keepdims=False)
        pieces.append(lax.ppermute(send, axes, [(k, (k + shift) % n) for k in range(n)]))
    return jnp.take(jnp.stack(pieces), (me - jnp.arange(n)) % n, axis=0)


def shards(factors, occ_energy, vir_energy, slab_orbitals, pair_list, pair_state, state_shift):
    n_zl = lax.axis_size("zl")
    n_y = lax.axis_size("y")
    n_x = lax.axis_size("x")
    n_zh = lax.axis_size("zh")
    n_core = lax.axis_size("core")
    n_row = n_zl * n_y
    n_col = n_x * n_zh * n_core
    local_aux, nocc, nvir = factors.shape
    rows_a = nvir // n_row
    cols_b = nvir // n_col
    row_index = lax.axis_index("zl") * n_y + lax.axis_index("y")
    col_index = (lax.axis_index("x") * n_zh + lax.axis_index("zh")) * n_core + lax.axis_index("core")
    spread_a = lax.all_to_all(
        factors.reshape(local_aux, nocc, n_row, rows_a), ("zl", "y"), split_axis=2, concat_axis=0, tiled=True
    )
    spread_a = spread_a.reshape(n_row * local_aux, nocc, rows_a)
    other_a = lax.ppermute(spread_a, "zh", [(k, (k + 1) % n_zh) for k in range(n_zh)])
    spread_b = permute_exchange(factors.reshape(local_aux, nocc, n_col, cols_b), ("x", "zh", "core"), col_index, n_col)
    other_a, spread_b = lax.optimization_barrier((other_a, spread_b))
    first_zh = lax.axis_index("zh") == 0
    pair_a = jnp.where(first_zh, jnp.stack([spread_a, other_a]), jnp.stack([other_a, spread_a]))
    block_a = lax.all_gather(pair_a, ("x", "core"), axis=0, tiled=True)
    spread_b = spread_b.reshape(n_col * local_aux, nocc, cols_b)
    other_b = lax.ppermute(spread_b, "zl", [(k, (k + 1) % n_zl) for k in range(n_zl)])
    me_zl = lax.axis_index("zl")
    block_b = jnp.zeros((n_zl, n_y) + spread_b.shape, spread_b.dtype)
    block_b = ring_into(block_b, me_zl, spread_b, "y")
    block_b = ring_into(block_b, (me_zl + 1) % n_zl, other_b, "y")
    block_a = block_a.reshape(n_x, n_core, n_zh, n_zl, n_y, local_aux, nocc, rows_a)
    block_b = block_b.reshape(n_zl, n_y, n_x, n_zh, n_core, local_aux, nocc, cols_b)
    gram = jnp.einsum(
        "xchzypia,zyxhcpjb->ijab",
        block_a,
        block_b,
        preferred_element_type=jnp.float32,
    ).reshape(nocc * nocc, rows_a, cols_b)
    first = pair_list[:, 0]
    second = pair_list[:, 1]
    kernel = jnp.take(gram, first * nocc + second, axis=0)
    vir_a = lax.dynamic_slice_in_dim(vir_energy, row_index * rows_a, rows_a)
    vir_b = lax.dynamic_slice_in_dim(vir_energy, col_index * cols_b, cols_b)
    e_first = occ_energy[slab_orbitals[first]]
    e_second = occ_energy[slab_orbitals[second]]
    shift = state_shift[pair_state]
    denom = (
        (vir_a[None, :, None] + vir_b[None, None, :])
        - e_first[:, None, None]
        - e_second[:, None, None]
        + shift[:, None, None]
    )
    return -kernel / denom


def solution(mesh):
    n_row, n_col = mesh.devices.shape
    sub = Mesh(mesh.devices.reshape(2, n_row // 2, n_col // 4, 2, 2), ("zl", "y", "x", "zh", "core"))
    placed = (P(("zl", "y", "x", "zh", "core"), None, None), P(), P(), P(), P(), P(), P())
    return jax.shard_map(
        shards, mesh=sub, in_specs=placed, out_specs=P(None, ("zl", "y"), ("x", "zh", "core")), check_vma=False
    )
```

```python
import jax
import jax.numpy as jnp
from jax import lax
from jax.sharding import Mesh, PartitionSpec as P


def ring_into(out, lead, shard, axis, mirror=None):
    n = lax.axis_size(axis)
    me = lax.axis_index(axis)
    right = [(k, (k + 1) % n) for k in range(n)]
    left = [(k, (k - 1) % n) for k in range(n)]
    zeros = (0,) * shard.ndim

    def put(buf, piece, index, offset=0):
        start = (lead, index, offset) + zeros[1:]
        buf = lax.dynamic_update_slice(buf, piece[None, None], start)
        if mirror is not None:
            mirror_axis, mirror_lead = mirror
            m = lax.axis_size(mirror_axis)
            twin = lax.ppermute(piece, mirror_axis, [(k, (k + 1) % m) for k in range(m)])
            buf = lax.dynamic_update_slice(buf, twin[None, None], (mirror_lead, index, offset) + zeros[1:])
        return buf

    out = put(out, shard, me)
    go_right = go_left = shard
    steps = n // 2
    for step in range(1, steps + 1):
        if step < steps or n % 2 == 1:
            go_right = lax.ppermute(go_right, axis, right)
            go_left = lax.ppermute(go_left, axis, left)
            out = put(out, go_right, (me - step) % n)
            out = put(out, go_left, (me + step) % n)
        else:
            half = shard.shape[0] // 2
            from_left = lax.ppermute(go_right[:half], axis, right)
            from_right = lax.ppermute(go_left[half:], axis, left)
            out = put(out, from_left, (me - step) % n)
            out = put(out, from_right, (me - step) % n, half)
    return out


def shards(factors, occ_energy, vir_energy, slab_orbitals, pair_list, pair_state, state_shift):
    n_zl = lax.axis_size("zl")
    n_y = lax.axis_size("y")
    n_x = lax.axis_size("x")
    n_zh = lax.axis_size("zh")
    n_core = lax.axis_size("core")
    n_row = n_zl * n_y
    n_col = n_x * n_zh * n_core
    local_aux, nocc, nvir = factors.shape
    rows_a = nvir // n_row
    cols_b = nvir // n_col
    row_index = lax.axis_index("zl") * n_y + lax.axis_index("y")
    col_index = (lax.axis_index("x") * n_zh + lax.axis_index("zh")) * n_core + lax.axis_index("core")
    spread_a = lax.all_to_all(
        factors.reshape(local_aux, nocc, n_row, rows_a), ("zl", "y"), split_axis=2, concat_axis=0, tiled=True
    )
    spread_a = spread_a.reshape(n_row * local_aux, nocc, rows_a)
    other_a = lax.ppermute(spread_a, "zh", [(k, (k + 1) % n_zh) for k in range(n_zh)])
    spread_b = lax.all_to_all(
        factors.reshape(local_aux, nocc, n_col, cols_b), ("x", "zh", "core"), split_axis=2, concat_axis=0, tiled=True
    )
    other_a, spread_b = lax.optimization_barrier((other_a, spread_b))
    first_zh = lax.axis_index("zh") == 0
    pair_a = jnp.where(first_zh, jnp.stack([spread_a, other_a]), jnp.stack([other_a, spread_a]))
    me_core = lax.axis_index("core")
    block_a = jnp.zeros((n_core, n_x) + pair_a.shape, pair_a.dtype)
    block_a = ring_into(block_a, me_core, pair_a, "x", mirror=("core", (me_core + 1) % n_core))
    spread_b = spread_b.reshape(n_col * local_aux, nocc, cols_b)
    other_b = lax.ppermute(spread_b, "zl", [(k, (k + 1) % n_zl) for k in range(n_zl)])
    me_zl = lax.axis_index("zl")
    block_b = jnp.zeros((n_zl, n_y) + spread_b.shape, spread_b.dtype)
    block_b = ring_into(block_b, me_zl, spread_b, "y")
    block_b = ring_into(block_b, (me_zl + 1) % n_zl, other_b, "y")
    block_a = block_a.reshape(n_core, n_x, n_zh, n_zl, n_y, local_aux, nocc, rows_a)
    block_b = block_b.reshape(n_zl, n_y, n_x, n_zh, n_core, local_aux, nocc, cols_b)
    gram = jnp.einsum(
        "cxhzypia,zyxhcpjb->ijab",
        block_a,
        block_b,
        preferred_element_type=jnp.float32,
    ).reshape(nocc * nocc, rows_a, cols_b)
    first = pair_list[:, 0]
    second = pair_list[:, 1]
    kernel = jnp.take(gram, first * nocc + second, axis=0)
    vir_a = lax.dynamic_slice_in_dim(vir_energy, row_index * rows_a, rows_a)
    vir_b = lax.dynamic_slice_in_dim(vir_energy, col_index * cols_b, cols_b)
    e_first = occ_energy[slab_orbitals[first]]
    e_second = occ_energy[slab_orbitals[second]]
    shift = state_shift[pair_state]
    denom = (
        (vir_a[None, :, None] + vir_b[None, None, :])
        - e_first[:, None, None]
        - e_second[:, None, None]
        + shift[:, None, None]
    )
    return -kernel / denom


def solution(mesh):
    n_row, n_col = mesh.devices.shape
    sub = Mesh(mesh.devices.reshape(2, n_row // 2, n_col // 4, 2, 2), ("zl", "y", "x", "zh", "core"))
    placed = (P(("zl", "y", "x", "zh", "core"), None, None), P(), P(), P(), P(), P(), P())
    return jax.shard_map(
        shards, mesh=sub, in_specs=placed, out_specs=P(None, ("zl", "y"), ("x", "zh", "core")), check_vma=False
    )
```

```python
import jax
import jax.numpy as jnp
from jax import lax
from jax.sharding import Mesh, PartitionSpec as P


def ring_into(out, lead, shard, axis):
    n = lax.axis_size(axis)
    me = lax.axis_index(axis)
    right = [(k, (k + 1) % n) for k in range(n)]
    left = [(k, (k - 1) % n) for k in range(n)]
    zeros = (0,) * shard.ndim

    def put(buf, piece, index, offset=0):
        start = (lead, index, offset) + zeros[1:]
        return lax.dynamic_update_slice(buf, piece[None, None], start)

    out = put(out, shard, me)
    go_right = go_left = shard
    steps = n // 2
    for step in range(1, steps + 1):
        if step < steps or n % 2 == 1:
            go_right = lax.ppermute(go_right, axis, right)
            go_left = lax.ppermute(go_left, axis, left)
            out = put(out, go_right, (me - step) % n)
            out = put(out, go_left, (me + step) % n)
        else:
            half = shard.shape[0] // 2
            from_left = lax.ppermute(go_right[:half], axis, right)
            from_right = lax.ppermute(go_left[half:], axis, left)
            out = put(out, from_left, (me - step) % n)
            out = put(out, from_right, (me - step) % n, half)
    return out


def shards(factors, occ_energy, vir_energy, slab_orbitals, pair_list, pair_state, state_shift):
    n_zl = lax.axis_size("zl")
    n_y = lax.axis_size("y")
    n_x = lax.axis_size("x")
    n_zh = lax.axis_size("zh")
    n_core = lax.axis_size("core")
    n_row = n_zl * n_y
    n_col = n_x * n_zh * n_core
    local_aux, nocc, nvir = factors.shape
    rows_a = nvir // n_row
    cols_b = nvir // n_col
    row_index = lax.axis_index("zl") * n_y + lax.axis_index("y")
    col_index = (lax.axis_index("x") * n_zh + lax.axis_index("zh")) * n_core + lax.axis_index("core")
    n_chunks = 2
    chunk = local_aux // n_chunks
    gram = None
    for c in range(n_chunks):
        part = lax.slice_in_dim(factors, c * chunk, (c + 1) * chunk, axis=0)
        spread_a = lax.all_to_all(
            part.reshape(chunk, nocc, n_row, rows_a), ("zl", "y"), split_axis=2, concat_axis=0, tiled=True
        )
        spread_a = spread_a.reshape(n_row * chunk, nocc, rows_a)
        other_a = lax.ppermute(spread_a, "zh", [(k, (k + 1) % n_zh) for k in range(n_zh)])
        spread_b = lax.all_to_all(
            part.reshape(chunk, nocc, n_col, cols_b), ("x", "zh", "core"), split_axis=2, concat_axis=0, tiled=True
        )
        other_a, spread_b = lax.optimization_barrier((other_a, spread_b))
        first_zh = lax.axis_index("zh") == 0
        pair_a = jnp.where(first_zh, jnp.stack([spread_a, other_a]), jnp.stack([other_a, spread_a]))
        block_a = lax.all_gather(pair_a, ("x", "core"), axis=0, tiled=True)
        spread_b = spread_b.reshape(n_col * chunk, nocc, cols_b)
        other_b = lax.ppermute(spread_b, "zl", [(k, (k + 1) % n_zl) for k in range(n_zl)])
        me_zl = lax.axis_index("zl")
        block_b = jnp.zeros((n_zl, n_y) + spread_b.shape, spread_b.dtype)
        block_b = ring_into(block_b, me_zl, spread_b, "y")
        block_b = ring_into(block_b, (me_zl + 1) % n_zl, other_b, "y")
        block_a = block_a.reshape(n_x, n_core, n_zh, n_zl, n_y, chunk, nocc, rows_a)
        block_b = block_b.reshape(n_zl, n_y, n_x, n_zh, n_core, chunk, nocc, cols_b)
        piece = jnp.einsum(
            "xchzypia,zyxhcpjb->ijab",
            block_a,
            block_b,
            preferred_element_type=jnp.float32,
        ).reshape(nocc * nocc, rows_a, cols_b)
        gram = piece if gram is None else gram + piece
    first = pair_list[:, 0]
    second = pair_list[:, 1]
    kernel = jnp.take(gram, first * nocc + second, axis=0)
    vir_a = lax.dynamic_slice_in_dim(vir_energy, row_index * rows_a, rows_a)
    vir_b = lax.dynamic_slice_in_dim(vir_energy, col_index * cols_b, cols_b)
    e_first = occ_energy[slab_orbitals[first]]
    e_second = occ_energy[slab_orbitals[second]]
    shift = state_shift[pair_state]
    denom = (
        (vir_a[None, :, None] + vir_b[None, None, :])
        - e_first[:, None, None]
        - e_second[:, None, None]
        + shift[:, None, None]
    )
    return -kernel / denom


def solution(mesh):
    n_row, n_col = mesh.devices.shape
    sub = Mesh(mesh.devices.reshape(2, n_row // 2, n_col // 4, 2, 2), ("zl", "y", "x", "zh", "core"))
    placed = (P(("zl", "y", "x", "zh", "core"), None, None), P(), P(), P(), P(), P(), P())
    return jax.shard_map(
        shards, mesh=sub, in_specs=placed, out_specs=P(None, ("zl", "y"), ("x", "zh", "core")), check_vma=False
    )
```

```python
import jax
import jax.numpy as jnp
from jax import lax
from jax.sharding import Mesh, PartitionSpec as P


def ring_into(out, lead, shard, axis):
    n = lax.axis_size(axis)
    me = lax.axis_index(axis)
    right = [(k, (k + 1) % n) for k in range(n)]
    left = [(k, (k - 1) % n) for k in range(n)]
    zeros = (0,) * shard.ndim

    def put(buf, piece, index, offset=0):
        start = (lead, index, offset) + zeros[1:]
        return lax.dynamic_update_slice(buf, piece[None, None], start)

    out = put(out, shard, me)
    go_right = go_left = shard
    steps = n // 2
    for step in range(1, steps + 1):
        if step < steps or n % 2 == 1:
            go_right = lax.ppermute(go_right, axis, right)
            go_left = lax.ppermute(go_left, axis, left)
            out = put(out, go_right, (me - step) % n)
            out = put(out, go_left, (me + step) % n)
        else:
            half = shard.shape[0] // 2
            from_left = lax.ppermute(go_right[:half], axis, right)
            from_right = lax.ppermute(go_left[half:], axis, left)
            out = put(out, from_left, (me - step) % n)
            out = put(out, from_right, (me - step) % n, half)
    return out


def shards(factors, occ_energy, vir_energy, slab_orbitals, pair_list, pair_state, state_shift):
    n_zl = lax.axis_size("zl")
    n_y = lax.axis_size("y")
    n_x = lax.axis_size("x")
    n_zh = lax.axis_size("zh")
    n_core = lax.axis_size("core")
    n_row = n_zl * n_y
    n_col = n_x * n_zh * n_core
    local_aux, nocc, nvir = factors.shape
    rows_a = nvir // n_row
    cols_b = nvir // n_col
    row_index = lax.axis_index("zl") * n_y + lax.axis_index("y")
    col_index = (lax.axis_index("x") * n_zh + lax.axis_index("zh")) * n_core + lax.axis_index("core")
    spread_a = lax.all_to_all(
        factors.reshape(local_aux, nocc, n_row, rows_a), ("zl", "y"), split_axis=2, concat_axis=0, tiled=True
    )
    spread_a = spread_a.reshape(n_row * local_aux, nocc, rows_a)
    block_a = lax.all_gather(spread_a, ("x", "zh", "core"), axis=0, tiled=True)
    spread_b = lax.all_to_all(
        factors.reshape(local_aux, nocc, n_col, cols_b), ("x", "zh", "core"), split_axis=2, concat_axis=0, tiled=True
    )
    spread_b = spread_b.reshape(n_col * local_aux, nocc, cols_b)
    other_b = lax.ppermute(spread_b, "zl", [(k, (k + 1) % n_zl) for k in range(n_zl)])
    me_zl = lax.axis_index("zl")
    block_b = jnp.zeros((n_zl, n_y) + spread_b.shape, spread_b.dtype)
    block_b = ring_into(block_b, me_zl, spread_b, "y")
    block_b = ring_into(block_b, (me_zl + 1) % n_zl, other_b, "y")
    block_a = block_a.reshape(n_x, n_zh, n_core, n_zl, n_y, local_aux, nocc, rows_a)
    block_b = block_b.reshape(n_zl, n_y, n_x, n_zh, n_core, local_aux, nocc, cols_b)
    gram = jnp.einsum(
        "xhczypia,zyxhcpjb->ijab",
        block_a,
        block_b,
        preferred_element_type=jnp.float32,
    ).reshape(nocc * nocc, rows_a, cols_b)
    first = pair_list[:, 0]
    second = pair_list[:, 1]
    kernel = jnp.take(gram, first * nocc + second, axis=0)
    vir_a = lax.dynamic_slice_in_dim(vir_energy, row_index * rows_a, rows_a)
    vir_b = lax.dynamic_slice_in_dim(vir_energy, col_index * cols_b, cols_b)
    e_first = occ_energy[slab_orbitals[first]]
    e_second = occ_energy[slab_orbitals[second]]
    shift = state_shift[pair_state]
    denom = (
        (vir_a[None, :, None] + vir_b[None, None, :])
        - e_first[:, None, None]
        - e_second[:, None, None]
        + shift[:, None, None]
    )
    return -kernel / denom


def solution(mesh):
    n_row, n_col = mesh.devices.shape
    sub = Mesh(mesh.devices.reshape(2, n_row // 2, n_col // 4, 2, 2), ("zl", "y", "x", "zh", "core"))
    placed = (P(("zl", "y", "x", "zh", "core"), None, None), P(), P(), P(), P(), P(), P())
    return jax.shard_map(
        shards, mesh=sub, in_specs=placed, out_specs=P(None, ("zl", "y"), ("x", "zh", "core")), check_vma=False
    )
```

```python
import jax
import jax.numpy as jnp
from jax import lax
from jax.sharding import Mesh, PartitionSpec as P


def ring_into(out, lead, shard, axis):
    n = lax.axis_size(axis)
    me = lax.axis_index(axis)
    right = [(k, (k + 1) % n) for k in range(n)]
    left = [(k, (k - 1) % n) for k in range(n)]
    zeros = (0,) * shard.ndim

    def put(buf, piece, index, offset=0):
        start = (lead, index, offset) + zeros[1:]
        return lax.dynamic_update_slice(buf, piece[None, None], start)

    out = put(out, shard, me)
    go_right = go_left = shard
    steps = n // 2
    for step in range(1, steps + 1):
        if step < steps or n % 2 == 1:
            go_right = lax.ppermute(go_right, axis, right)
            go_left = lax.ppermute(go_left, axis, left)
            out = put(out, go_right, (me - step) % n)
            out = put(out, go_left, (me + step) % n)
        else:
            half = shard.shape[0] // 2
            from_left = lax.ppermute(go_right[:half], axis, right)
            from_right = lax.ppermute(go_left[half:], axis, left)
            out = put(out, from_left, (me - step) % n)
            out = put(out, from_right, (me - step) % n, half)
    return out


def shards(factors, occ_energy, vir_energy, slab_orbitals, pair_list, pair_state, state_shift):
    n_zl = lax.axis_size("zl")
    n_y = lax.axis_size("y")
    n_x = lax.axis_size("x")
    n_zh = lax.axis_size("zh")
    n_core = lax.axis_size("core")
    n_row = n_zl * n_y
    n_col = n_x * n_zh * n_core
    local_aux, nocc, nvir = factors.shape
    rows_a = nvir // n_row
    cols_b = nvir // n_col
    row_index = lax.axis_index("zl") * n_y + lax.axis_index("y")
    col_index = (lax.axis_index("x") * n_zh + lax.axis_index("zh")) * n_core + lax.axis_index("core")
    spread_a = lax.all_to_all(
        factors.reshape(local_aux, nocc, n_row, rows_a), ("zl", "y"), split_axis=2, concat_axis=0, tiled=True
    )
    spread_a = spread_a.reshape(n_row * local_aux, nocc, rows_a)
    spread_b = lax.all_to_all(
        factors.reshape(local_aux, nocc, n_col, cols_b), ("x", "zh", "core"), split_axis=2, concat_axis=0, tiled=True
    )
    spread_b = spread_b.reshape(n_col * local_aux, nocc, cols_b)
    other_b = lax.ppermute(spread_b, "zl", [(k, (k + 1) % n_zl) for k in range(n_zl)])
    me_zl = lax.axis_index("zl")
    block_b = jnp.zeros((n_zl, n_y) + spread_b.shape, spread_b.dtype)
    block_b = ring_into(block_b, me_zl, spread_b, "y")
    block_b = ring_into(block_b, (me_zl + 1) % n_zl, other_b, "y")
    block_b = block_b.reshape(n_zl, n_y, n_x, n_zh, n_core, local_aux, nocc, cols_b)
    n_half = 2
    width = rows_a // n_half
    grams = []
    for h in range(n_half):
        part = lax.slice_in_dim(spread_a, h * width, (h + 1) * width, axis=2)
        block_a = lax.all_gather(part, ("x", "zh", "core"), axis=0, tiled=True)
        block_a = block_a.reshape(n_x, n_zh, n_core, n_zl, n_y, local_aux, nocc, width)
        grams.append(
            jnp.einsum("xhczypia,zyxhcpjb->ijab", block_a, block_b, preferred_element_type=jnp.float32)
        )
    gram = jnp.concatenate(grams, axis=2).reshape(nocc * nocc, rows_a, cols_b)
    first = pair_list[:, 0]
    second = pair_list[:, 1]
    kernel = jnp.take(gram, first * nocc + second, axis=0)
    vir_a = lax.dynamic_slice_in_dim(vir_energy, row_index * rows_a, rows_a)
    vir_b = lax.dynamic_slice_in_dim(vir_energy, col_index * cols_b, cols_b)
    e_first = occ_energy[slab_orbitals[first]]
    e_second = occ_energy[slab_orbitals[second]]
    shift = state_shift[pair_state]
    denom = (
        (vir_a[None, :, None] + vir_b[None, None, :])
        - e_first[:, None, None]
        - e_second[:, None, None]
        + shift[:, None, None]
    )
    return -kernel / denom


def solution(mesh):
    n_row, n_col = mesh.devices.shape
    sub = Mesh(mesh.devices.reshape(2, n_row // 2, n_col // 4, 2, 2), ("zl", "y", "x", "zh", "core"))
    placed = (P(("zl", "y", "x", "zh", "core"), None, None), P(), P(), P(), P(), P(), P())
    return jax.shard_map(
        shards, mesh=sub, in_specs=placed, out_specs=P(None, ("zl", "y"), ("x", "zh", "core")), check_vma=False
    )
```

```python
import jax
import jax.numpy as jnp
from jax import lax
from jax.sharding import Mesh, PartitionSpec as P


def ring_into(out, lead, shard, axis):
    n = lax.axis_size(axis)
    me = lax.axis_index(axis)
    right = [(k, (k + 1) % n) for k in range(n)]
    left = [(k, (k - 1) % n) for k in range(n)]
    zeros = (0,) * shard.ndim

    def put(buf, piece, index, offset=0):
        start = (lead, index, offset) + zeros[1:]
        return lax.dynamic_update_slice(buf, piece[None, None], start)

    out = put(out, shard, me)
    go_right = go_left = shard
    steps = n // 2
    for step in range(1, steps + 1):
        if step < steps or n % 2 == 1:
            go_right = lax.ppermute(go_right, axis, right)
            go_left = lax.ppermute(go_left, axis, left)
            out = put(out, go_right, (me - step) % n)
            out = put(out, go_left, (me + step) % n)
        else:
            half = shard.shape[0] // 2
            from_left = lax.ppermute(go_right[:half], axis, right)
            from_right = lax.ppermute(go_left[half:], axis, left)
            out = put(out, from_left, (me - step) % n)
            out = put(out, from_right, (me - step) % n, half)
    return out


def shards(factors, occ_energy, vir_energy, slab_orbitals, pair_list, pair_state, state_shift):
    n_zl = lax.axis_size("zl")
    n_y = lax.axis_size("y")
    n_x = lax.axis_size("x")
    n_zh = lax.axis_size("zh")
    n_core = lax.axis_size("core")
    n_row = n_zl * n_y
    n_col = n_x * n_zh * n_core
    local_aux, nocc, nvir = factors.shape
    rows_a = nvir // n_row
    cols_b = nvir // n_col
    row_index = lax.axis_index("zl") * n_y + lax.axis_index("y")
    col_index = (lax.axis_index("x") * n_zh + lax.axis_index("zh")) * n_core + lax.axis_index("core")
    spread_a = lax.all_to_all(
        factors.reshape(local_aux, nocc, n_row, rows_a), ("zl", "y"), split_axis=2, concat_axis=0, tiled=True
    )
    spread_a = spread_a.reshape(n_row * local_aux, nocc, rows_a)
    pair_a = lax.all_gather(spread_a, "zh", axis=0, tiled=False)
    spread_b = lax.all_to_all(
        factors.reshape(local_aux, nocc, n_col, cols_b), ("x", "zh", "core"), split_axis=2, concat_axis=0, tiled=True
    )
    pair_a, spread_b = lax.optimization_barrier((pair_a, spread_b))
    block_a = lax.all_gather(pair_a, ("x", "core"), axis=0, tiled=True)
    spread_b = spread_b.reshape(n_col * local_aux, nocc, cols_b)
    other_b = lax.ppermute(spread_b, "zl", [(k, (k + 1) % n_zl) for k in range(n_zl)])
    me_zl = lax.axis_index("zl")
    block_b = jnp.zeros((n_zl, n_y) + spread_b.shape, spread_b.dtype)
    block_b = ring_into(block_b, me_zl, spread_b, "y")
    block_b = ring_into(block_b, (me_zl + 1) % n_zl, other_b, "y")
    block_a = block_a.reshape(n_x, n_core, n_zh, n_zl, n_y, local_aux, nocc, rows_a)
    block_b = block_b.reshape(n_zl, n_y, n_x, n_zh, n_core, local_aux, nocc, cols_b)
    gram = jnp.einsum(
        "xchzypia,zyxhcpjb->ijab",
        block_a,
        block_b,
        preferred_element_type=jnp.float32,
    ).reshape(nocc * nocc, rows_a, cols_b)
    first = pair_list[:, 0]
    second = pair_list[:, 1]
    kernel = jnp.take(gram, first * nocc + second, axis=0)
    vir_a = lax.dynamic_slice_in_dim(vir_energy, row_index * rows_a, rows_a)
    vir_b = lax.dynamic_slice_in_dim(vir_energy, col_index * cols_b, cols_b)
    e_first = occ_energy[slab_orbitals[first]]
    e_second = occ_energy[slab_orbitals[second]]
    shift = state_shift[pair_state]
    denom = (
        (vir_a[None, :, None] + vir_b[None, None, :])
        - e_first[:, None, None]
        - e_second[:, None, None]
        + shift[:, None, None]
    )
    return -kernel / denom


def solution(mesh):
    n_row, n_col = mesh.devices.shape
    sub = Mesh(mesh.devices.reshape(2, n_row // 2, n_col // 4, 2, 2), ("zl", "y", "x", "zh", "core"))
    placed = (P(("zl", "y", "x", "zh", "core"), None, None), P(), P(), P(), P(), P(), P())
    return jax.shard_map(
        shards, mesh=sub, in_specs=placed, out_specs=P(None, ("zl", "y"), ("x", "zh", "core")), check_vma=False
    )
```

```python
import jax
import jax.numpy as jnp
from jax import lax
from jax.sharding import Mesh, PartitionSpec as P


def ring_into(out, lead, shard, axis):
    n = lax.axis_size(axis)
    me = lax.axis_index(axis)
    right = [(k, (k + 1) % n) for k in range(n)]
    left = [(k, (k - 1) % n) for k in range(n)]
    zeros = (0,) * shard.ndim

    def put(buf, piece, index, offset=0):
        start = (lead, index, offset) + zeros[1:]
        return lax.dynamic_update_slice(buf, piece[None, None], start)

    out = put(out, shard, me)
    go_right = go_left = shard
    steps = n // 2
    for step in range(1, steps + 1):
        if step < steps or n % 2 == 1:
            go_right = lax.ppermute(go_right, axis, right)
            go_left = lax.ppermute(go_left, axis, left)
            out = put(out, go_right, (me - step) % n)
            out = put(out, go_left, (me + step) % n)
        else:
            half = shard.shape[0] // 2
            from_left = lax.ppermute(go_right[:half], axis, right)
            from_right = lax.ppermute(go_left[half:], axis, left)
            out = put(out, from_left, (me - step) % n)
            out = put(out, from_right, (me - step) % n, half)
    return out


def shards(factors, occ_energy, vir_energy, slab_orbitals, pair_list, pair_state, state_shift):
    n_zl = lax.axis_size("zl")
    n_y = lax.axis_size("y")
    n_x = lax.axis_size("x")
    n_zh = lax.axis_size("zh")
    n_core = lax.axis_size("core")
    n_row = n_zl * n_y
    n_col = n_x * n_zh * n_core
    local_aux, nocc, nvir = factors.shape
    rows_a = nvir // n_row
    cols_b = nvir // n_col
    row_index = lax.axis_index("zl") * n_y + lax.axis_index("y")
    col_index = (lax.axis_index("x") * n_zh + lax.axis_index("zh")) * n_core + lax.axis_index("core")
    spread_a = lax.all_to_all(
        factors.reshape(local_aux, nocc, n_row, rows_a), ("zl", "y"), split_axis=2, concat_axis=0, tiled=True
    )
    spread_a = spread_a.reshape(n_row * local_aux, nocc, rows_a)
    other_a = lax.ppermute(spread_a, "zh", [(k, (k + 1) % n_zh) for k in range(n_zh)])
    by_chip = lax.all_to_all(
        factors.reshape(local_aux, nocc, n_x * n_zh, n_core, cols_b), ("x", "zh"), split_axis=2, concat_axis=0, tiled=True
    )
    other_a, by_chip = lax.optimization_barrier((other_a, by_chip))
    me_core = lax.axis_index("core")
    by_chip = by_chip.reshape(n_x * n_zh * local_aux, nocc, n_core, cols_b)
    keep = lax.dynamic_index_in_dim(by_chip, me_core, 2, keepdims=False)
    give = lax.dynamic_index_in_dim(by_chip, (me_core + 1) % n_core, 2, keepdims=False)
    got = lax.ppermute(give, "core", [(k, (k + 1) % n_core) for k in range(n_core)])
    spread_b = jnp.where(me_core == 0, jnp.stack([keep, got]), jnp.stack([got, keep]))
    first_zh = lax.axis_index("zh") == 0
    pair_a = jnp.where(first_zh, jnp.stack([spread_a, other_a]), jnp.stack([other_a, spread_a]))
    block_a = lax.all_gather(pair_a, ("x", "core"), axis=0, tiled=True)
    spread_b = spread_b.reshape(n_col * local_aux, nocc, cols_b)
    other_b = lax.ppermute(spread_b, "zl", [(k, (k + 1) % n_zl) for k in range(n_zl)])
    me_zl = lax.axis_index("zl")
    block_b = jnp.zeros((n_zl, n_y) + spread_b.shape, spread_b.dtype)
    block_b = ring_into(block_b, me_zl, spread_b, "y")
    block_b = ring_into(block_b, (me_zl + 1) % n_zl, other_b, "y")
    block_a = block_a.reshape(n_x, n_core, n_zh, n_zl, n_y, local_aux, nocc, rows_a)
    block_b = block_b.reshape(n_zl, n_y, n_core, n_x, n_zh, local_aux, nocc, cols_b)
    gram = jnp.einsum(
        "xchzypia,zycxhpjb->ijab",
        block_a,
        block_b,
        preferred_element_type=jnp.float32,
    ).reshape(nocc * nocc, rows_a, cols_b)
    first = pair_list[:, 0]
    second = pair_list[:, 1]
    kernel = jnp.take(gram, first * nocc + second, axis=0)
    vir_a = lax.dynamic_slice_in_dim(vir_energy, row_index * rows_a, rows_a)
    vir_b = lax.dynamic_slice_in_dim(vir_energy, col_index * cols_b, cols_b)
    e_first = occ_energy[slab_orbitals[first]]
    e_second = occ_energy[slab_orbitals[second]]
    shift = state_shift[pair_state]
    denom = (
        (vir_a[None, :, None] + vir_b[None, None, :])
        - e_first[:, None, None]
        - e_second[:, None, None]
        + shift[:, None, None]
    )
    return -kernel / denom


def solution(mesh):
    n_row, n_col = mesh.devices.shape
    sub = Mesh(mesh.devices.reshape(2, n_row // 2, n_col // 4, 2, 2), ("zl", "y", "x", "zh", "core"))
    placed = (P(("zl", "y", "x", "zh", "core"), None, None), P(), P(), P(), P(), P(), P())
    return jax.shard_map(
        shards, mesh=sub, in_specs=placed, out_specs=P(None, ("zl", "y"), ("x", "zh", "core")), check_vma=False
    )
```

```python
import jax
import jax.numpy as jnp
from jax import lax
from jax.sharding import Mesh, PartitionSpec as P


def ring_into(out, lead, shard, axis):
    n = lax.axis_size(axis)
    me = lax.axis_index(axis)
    right = [(k, (k + 1) % n) for k in range(n)]
    left = [(k, (k - 1) % n) for k in range(n)]
    zeros = (0,) * shard.ndim

    def put(buf, piece, index, offset=0):
        start = (lead, index, offset) + zeros[1:]
        return lax.dynamic_update_slice(buf, piece[None, None], start)

    out = put(out, shard, me)
    go_right = go_left = shard
    steps = n // 2
    for step in range(1, steps + 1):
        if step < steps or n % 2 == 1:
            go_right = lax.ppermute(go_right, axis, right)
            go_left = lax.ppermute(go_left, axis, left)
            out = put(out, go_right, (me - step) % n)
            out = put(out, go_left, (me + step) % n)
        else:
            half = shard.shape[0] // 2
            from_left = lax.ppermute(go_right[:half], axis, right)
            from_right = lax.ppermute(go_left[half:], axis, left)
            out = put(out, from_left, (me - step) % n)
            out = put(out, from_right, (me - step) % n, half)
    return out


def shards(factors, occ_energy, vir_energy, slab_orbitals, pair_list, pair_state, state_shift):
    n_zl = lax.axis_size("zl")
    n_y = lax.axis_size("y")
    n_x = lax.axis_size("x")
    n_zh = lax.axis_size("zh")
    n_core = lax.axis_size("core")
    n_row = n_zl * n_y
    n_col = n_x * n_zh * n_core
    local_aux, nocc, nvir = factors.shape
    rows_a = nvir // n_row
    cols_b = nvir // n_col
    row_index = lax.axis_index("zl") * n_y + lax.axis_index("y")
    col_index = (lax.axis_index("x") * n_zh + lax.axis_index("zh")) * n_core + lax.axis_index("core")
    spread_a = lax.all_to_all(
        factors.reshape(local_aux, nocc, n_row, rows_a), ("zl", "y"), split_axis=2, concat_axis=0, tiled=True
    )
    spread_a = spread_a.reshape(n_row * local_aux, nocc, rows_a)
    other_a = lax.ppermute(spread_a, "zh", [(k, (k + 1) % n_zh) for k in range(n_zh)])
    by_chip = lax.all_to_all(
        factors.reshape(local_aux, nocc, n_x * n_zh, n_core, cols_b), ("x", "zh"), split_axis=2, concat_axis=0, tiled=True
    )
    twice_a = jnp.stack([spread_a, spread_a])
    other_a, by_chip, twice_a = lax.optimization_barrier((other_a, by_chip, twice_a))
    me_core = lax.axis_index("core")
    by_chip = by_chip.reshape(n_x * n_zh * local_aux, nocc, n_core, cols_b)
    keep = lax.dynamic_index_in_dim(by_chip, me_core, 2, keepdims=False)
    give = lax.dynamic_index_in_dim(by_chip, (me_core + 1) % n_core, 2, keepdims=False)
    got = lax.ppermute(give, "core", [(k, (k + 1) % n_core) for k in range(n_core)])
    spread_b = jnp.where(me_core == 0, jnp.stack([keep, got]), jnp.stack([got, keep]))
    other_slot = (lax.axis_index("zh") + 1) % n_zh
    pair_a = lax.dynamic_update_index_in_dim(twice_a, other_a, other_slot, 0)
    block_a = lax.all_gather(pair_a, ("x", "core"), axis=0, tiled=True)
    spread_b = spread_b.reshape(n_col * local_aux, nocc, cols_b)
    other_b = lax.ppermute(spread_b, "zl", [(k, (k + 1) % n_zl) for k in range(n_zl)])
    me_zl = lax.axis_index("zl")
    block_b = jnp.zeros((n_zl, n_y) + spread_b.shape, spread_b.dtype)
    block_b = ring_into(block_b, me_zl, spread_b, "y")
    block_b = ring_into(block_b, (me_zl + 1) % n_zl, other_b, "y")
    block_a = block_a.reshape(n_x, n_core, n_zh, n_zl, n_y, local_aux, nocc, rows_a)
    block_b = block_b.reshape(n_zl, n_y, n_core, n_x, n_zh, local_aux, nocc, cols_b)
    gram = jnp.einsum(
        "xchzypia,zycxhpjb->ijab",
        block_a,
        block_b,
        preferred_element_type=jnp.float32,
    ).reshape(nocc * nocc, rows_a, cols_b)
    first = pair_list[:, 0]
    second = pair_list[:, 1]
    kernel = jnp.take(gram, first * nocc + second, axis=0)
    vir_a = lax.dynamic_slice_in_dim(vir_energy, row_index * rows_a, rows_a)
    vir_b = lax.dynamic_slice_in_dim(vir_energy, col_index * cols_b, cols_b)
    e_first = occ_energy[slab_orbitals[first]]
    e_second = occ_energy[slab_orbitals[second]]
    shift = state_shift[pair_state]
    denom = (
        (vir_a[None, :, None] + vir_b[None, None, :])
        - e_first[:, None, None]
        - e_second[:, None, None]
        + shift[:, None, None]
    )
    return -kernel / denom


def solution(mesh):
    n_row, n_col = mesh.devices.shape
    sub = Mesh(mesh.devices.reshape(2, n_row // 2, n_col // 4, 2, 2), ("zl", "y", "x", "zh", "core"))
    placed = (P(("zl", "y", "x", "zh", "core"), None, None), P(), P(), P(), P(), P(), P())
    return jax.shard_map(
        shards, mesh=sub, in_specs=placed, out_specs=P(None, ("zl", "y"), ("x", "zh", "core")), check_vma=False
    )
```

```python
import jax
import jax.numpy as jnp
from jax import lax
from jax.sharding import Mesh, PartitionSpec as P


def ring_into(out, lead, shard, axis):
    n = lax.axis_size(axis)
    me = lax.axis_index(axis)
    right = [(k, (k + 1) % n) for k in range(n)]
    left = [(k, (k - 1) % n) for k in range(n)]
    zeros = (0,) * shard.ndim

    def put(buf, piece, index, offset=0):
        start = (lead, index, offset) + zeros[1:]
        return lax.dynamic_update_slice(buf, piece[None, None], start)

    out = put(out, shard, me)
    go_right = go_left = shard
    steps = n // 2
    for step in range(1, steps + 1):
        if step < steps or n % 2 == 1:
            go_right = lax.ppermute(go_right, axis, right)
            go_left = lax.ppermute(go_left, axis, left)
            out = put(out, go_right, (me - step) % n)
            out = put(out, go_left, (me + step) % n)
        else:
            half = shard.shape[0] // 2
            from_left = lax.ppermute(go_right[:half], axis, right)
            from_right = lax.ppermute(go_left[half:], axis, left)
            out = put(out, from_left, (me - step) % n)
            out = put(out, from_right, (me - step) % n, half)
    return out


def shards(factors, occ_energy, vir_energy, slab_orbitals, pair_list, pair_state, state_shift):
    n_zl = lax.axis_size("zl")
    n_y = lax.axis_size("y")
    n_x = lax.axis_size("x")
    n_zh = lax.axis_size("zh")
    n_core = lax.axis_size("core")
    n_row = n_zl * n_y
    n_col = n_x * n_zh * n_core
    local_aux, nocc, nvir = factors.shape
    rows_a = nvir // n_row
    cols_b = nvir // n_col
    row_index = lax.axis_index("zl") * n_y + lax.axis_index("y")
    col_index = (lax.axis_index("x") * n_zh + lax.axis_index("zh")) * n_core + lax.axis_index("core")
    spread_a = lax.all_to_all(factors, ("zl", "y"), split_axis=2, concat_axis=0, tiled=True)
    spread_a = spread_a.reshape(n_row * local_aux, nocc, rows_a)
    other_a = lax.ppermute(spread_a, "zh", [(k, (k + 1) % n_zh) for k in range(n_zh)])
    by_chip = lax.all_to_all(factors, ("x", "zh"), split_axis=2, concat_axis=0, tiled=True)
    other_a, by_chip = lax.optimization_barrier((other_a, by_chip))
    me_core = lax.axis_index("core")
    by_chip = by_chip.reshape(n_x * n_zh * local_aux, nocc, n_core, cols_b)
    keep = lax.dynamic_index_in_dim(by_chip, me_core, 2, keepdims=False)
    give = lax.dynamic_index_in_dim(by_chip, (me_core + 1) % n_core, 2, keepdims=False)
    got = lax.ppermute(give, "core", [(k, (k + 1) % n_core) for k in range(n_core)])
    spread_b = jnp.where(me_core == 0, jnp.stack([keep, got]), jnp.stack([got, keep]))
    first_zh = lax.axis_index("zh") == 0
    pair_a = jnp.where(first_zh, jnp.stack([spread_a, other_a]), jnp.stack([other_a, spread_a]))
    block_a = lax.all_gather(pair_a, ("x", "core"), axis=0, tiled=True)
    spread_b = spread_b.reshape(n_col * local_aux, nocc, cols_b)
    other_b = lax.ppermute(spread_b, "zl", [(k, (k + 1) % n_zl) for k in range(n_zl)])
    me_zl = lax.axis_index("zl")
    block_b = jnp.zeros((n_zl, n_y) + spread_b.shape, spread_b.dtype)
    block_b = ring_into(block_b, me_zl, spread_b, "y")
    block_b = ring_into(block_b, (me_zl + 1) % n_zl, other_b, "y")
    block_a = block_a.reshape(n_x, n_core, n_zh, n_zl, n_y, local_aux, nocc, rows_a)
    block_b = block_b.reshape(n_zl, n_y, n_core, n_x, n_zh, local_aux, nocc, cols_b)
    gram = jnp.einsum(
        "xchzypia,zycxhpjb->ijab",
        block_a,
        block_b,
        preferred_element_type=jnp.float32,
    ).reshape(nocc * nocc, rows_a, cols_b)
    first = pair_list[:, 0]
    second = pair_list[:, 1]
    kernel = jnp.take(gram, first * nocc + second, axis=0)
    vir_a = lax.dynamic_slice_in_dim(vir_energy, row_index * rows_a, rows_a)
    vir_b = lax.dynamic_slice_in_dim(vir_energy, col_index * cols_b, cols_b)
    e_first = occ_energy[slab_orbitals[first]]
    e_second = occ_energy[slab_orbitals[second]]
    shift = state_shift[pair_state]
    denom = (
        (vir_a[None, :, None] + vir_b[None, None, :])
        - e_first[:, None, None]
        - e_second[:, None, None]
        + shift[:, None, None]
    )
    return -kernel / denom


def solution(mesh):
    n_row, n_col = mesh.devices.shape
    sub = Mesh(mesh.devices.reshape(2, n_row // 2, n_col // 4, 2, 2), ("zl", "y", "x", "zh", "core"))
    placed = (P(("zl", "y", "x", "zh", "core"), None, None), P(), P(), P(), P(), P(), P())
    return jax.shard_map(
        shards, mesh=sub, in_specs=placed, out_specs=P(None, ("zl", "y"), ("x", "zh", "core")), check_vma=False
    )
```

```python
import jax
import jax.numpy as jnp
from jax import lax
from jax.sharding import Mesh, PartitionSpec as P


def ring_into(out, lead, shard, axis):
    n = lax.axis_size(axis)
    me = lax.axis_index(axis)
    right = [(k, (k + 1) % n) for k in range(n)]
    left = [(k, (k - 1) % n) for k in range(n)]
    zeros = (0,) * shard.ndim

    def put(buf, piece, index, offset=0):
        start = (lead, index, offset) + zeros[1:]
        return lax.dynamic_update_slice(buf, piece[None, None], start)

    out = put(out, shard, me)
    go_right = go_left = shard
    steps = n // 2
    for step in range(1, steps + 1):
        if step < steps or n % 2 == 1:
            go_right = lax.ppermute(go_right, axis, right)
            go_left = lax.ppermute(go_left, axis, left)
            out = put(out, go_right, (me - step) % n)
            out = put(out, go_left, (me + step) % n)
        else:
            half = shard.shape[0] // 2
            from_left = lax.ppermute(go_right[:half], axis, right)
            from_right = lax.ppermute(go_left[half:], axis, left)
            out = put(out, from_left, (me - step) % n)
            out = put(out, from_right, (me - step) % n, half)
    return out


def shards(factors, occ_energy, vir_energy, slab_orbitals, pair_list, pair_state, state_shift):
    n_zl = lax.axis_size("zl")
    n_y = lax.axis_size("y")
    n_x = lax.axis_size("x")
    n_zh = lax.axis_size("zh")
    n_core = lax.axis_size("core")
    n_row = n_zl * n_y
    n_col = n_x * n_zh * n_core
    local_aux, nocc, nvir = factors.shape
    rows_a = nvir // n_row
    cols_b = nvir // n_col
    row_index = lax.axis_index("zl") * n_y + lax.axis_index("y")
    col_index = (lax.axis_index("x") * n_zh + lax.axis_index("zh")) * n_core + lax.axis_index("core")
    spread_a = lax.all_to_all(
        factors.reshape(local_aux, nocc, n_row, rows_a), ("zl", "y"), split_axis=2, concat_axis=0, tiled=True
    )
    spread_a = spread_a.reshape(n_row * local_aux, nocc, rows_a)
    other_a = lax.ppermute(spread_a, "zh", [(k, (k + 1) % n_zh) for k in range(n_zh)])
    by_chip = lax.all_to_all(
        factors.reshape(local_aux, nocc, n_x * n_zh, n_core, cols_b), ("x", "zh"), split_axis=2, concat_axis=0, tiled=True
    )
    other_a, by_chip = lax.optimization_barrier((other_a, by_chip))
    me_core = lax.axis_index("core")
    by_chip = by_chip.reshape(n_x * n_zh * local_aux, nocc, n_core, cols_b)
    keep = lax.dynamic_index_in_dim(by_chip, me_core, 2, keepdims=False)
    give = lax.dynamic_index_in_dim(by_chip, (me_core + 1) % n_core, 2, keepdims=False)
    got = lax.ppermute(give, "core", [(k, (k + 1) % n_core) for k in range(n_core)])
    spread_b = jnp.where(me_core == 0, jnp.stack([keep, got]), jnp.stack([got, keep]))
    first_zh = lax.axis_index("zh") == 0
    pair_a = jnp.where(first_zh, jnp.stack([spread_a, other_a]), jnp.stack([other_a, spread_a]))
    block_a = lax.all_gather(pair_a, ("core", "x"), axis=0, tiled=True)
    spread_b = spread_b.reshape(n_col * local_aux, nocc, cols_b)
    other_b = lax.ppermute(spread_b, "zl", [(k, (k + 1) % n_zl) for k in range(n_zl)])
    me_zl = lax.axis_index("zl")
    block_b = jnp.zeros((n_zl, n_y) + spread_b.shape, spread_b.dtype)
    block_b = ring_into(block_b, me_zl, spread_b, "y")
    block_b = ring_into(block_b, (me_zl + 1) % n_zl, other_b, "y")
    block_a = block_a.reshape(n_core, n_x, n_zh, n_zl, n_y, local_aux, nocc, rows_a)
    block_b = block_b.reshape(n_zl, n_y, n_core, n_x, n_zh, local_aux, nocc, cols_b)
    gram = jnp.einsum(
        "cxhzypia,zycxhpjb->ijab",
        block_a,
        block_b,
        preferred_element_type=jnp.float32,
    ).reshape(nocc * nocc, rows_a, cols_b)
    first = pair_list[:, 0]
    second = pair_list[:, 1]
    kernel = jnp.take(gram, first * nocc + second, axis=0)
    vir_a = lax.dynamic_slice_in_dim(vir_energy, row_index * rows_a, rows_a)
    vir_b = lax.dynamic_slice_in_dim(vir_energy, col_index * cols_b, cols_b)
    e_first = occ_energy[slab_orbitals[first]]
    e_second = occ_energy[slab_orbitals[second]]
    shift = state_shift[pair_state]
    denom = (
        (vir_a[None, :, None] + vir_b[None, None, :])
        - e_first[:, None, None]
        - e_second[:, None, None]
        + shift[:, None, None]
    )
    return -kernel / denom


def solution(mesh):
    n_row, n_col = mesh.devices.shape
    sub = Mesh(mesh.devices.reshape(2, n_row // 2, n_col // 4, 2, 2), ("zl", "y", "x", "zh", "core"))
    placed = (P(("zl", "y", "x", "zh", "core"), None, None), P(), P(), P(), P(), P(), P())
    return jax.shard_map(
        shards, mesh=sub, in_specs=placed, out_specs=P(None, ("zl", "y"), ("x", "zh", "core")), check_vma=False
    )
```

```python
import jax
import jax.numpy as jnp
from jax import lax
from jax.sharding import Mesh, PartitionSpec as P


def ring_into(out, lead, shard, axis):
    n = lax.axis_size(axis)
    me = lax.axis_index(axis)
    right = [(k, (k + 1) % n) for k in range(n)]
    left = [(k, (k - 1) % n) for k in range(n)]
    zeros = (0,) * shard.ndim

    def put(buf, piece, index, offset=0):
        start = (lead, index, offset) + zeros[1:]
        return lax.dynamic_update_slice(buf, piece[None, None], start)

    out = put(out, shard, me)
    go_right = go_left = shard
    steps = n // 2
    for step in range(1, steps + 1):
        if step < steps or n % 2 == 1:
            go_right = lax.ppermute(go_right, axis, right)
            go_left = lax.ppermute(go_left, axis, left)
            out = put(out, go_right, (me - step) % n)
            out = put(out, go_left, (me + step) % n)
        else:
            half = shard.shape[0] // 2
            from_left = lax.ppermute(go_right[:half], axis, right)
            from_right = lax.ppermute(go_left[half:], axis, left)
            out = put(out, from_left, (me - step) % n)
            out = put(out, from_right, (me - step) % n, half)
    return out


def shards(factors, occ_energy, vir_energy, slab_orbitals, pair_list, pair_state, state_shift):
    n_zl = lax.axis_size("zl")
    n_y = lax.axis_size("y")
    n_x = lax.axis_size("x")
    n_zh = lax.axis_size("zh")
    n_core = lax.axis_size("core")
    n_row = n_zl * n_y
    n_col = n_x * n_zh * n_core
    local_aux, nocc, nvir = factors.shape
    rows_a = nvir // n_row
    cols_b = nvir // n_col
    row_index = lax.axis_index("zl") * n_y + lax.axis_index("y")
    col_index = (lax.axis_index("x") * n_zh + lax.axis_index("zh")) * n_core + lax.axis_index("core")
    spread_a = lax.all_to_all(
        factors.reshape(local_aux, nocc, n_row, rows_a), ("zl", "y"), split_axis=2, concat_axis=0, tiled=True
    )
    spread_a = spread_a.reshape(n_row * local_aux, nocc, rows_a)
    other_a = lax.ppermute(spread_a, "zh", [(k, (k + 1) % n_zh) for k in range(n_zh)])
    by_chip = lax.all_to_all(
        factors.reshape(local_aux, nocc, n_x * n_zh, n_core, cols_b), ("x", "zh"), split_axis=2, concat_axis=0, tiled=True
    )
    other_a, by_chip = lax.optimization_barrier((other_a, by_chip))
    me_core = lax.axis_index("core")
    by_chip = by_chip.reshape(n_x * n_zh * local_aux, nocc, n_core, cols_b)
    keep = lax.dynamic_index_in_dim(by_chip, me_core, 2, keepdims=False)
    give = lax.dynamic_index_in_dim(by_chip, (me_core + 1) % n_core, 2, keepdims=False)
    got = lax.ppermute(give, "core", [(k, (k + 1) % n_core) for k in range(n_core)])
    spread_b = jnp.where(me_core == 0, jnp.stack([keep, got]), jnp.stack([got, keep]))
    first_zh = lax.axis_index("zh") == 0
    pair_a = jnp.where(first_zh, jnp.stack([spread_a, other_a]), jnp.stack([other_a, spread_a]))
    block_a = lax.all_gather(pair_a, ("core", "x"), axis=0, tiled=True)
    spread_b = spread_b.reshape(n_col * local_aux, nocc, cols_b)
    other_b = lax.ppermute(spread_b, "zl", [(k, (k + 1) % n_zl) for k in range(n_zl)])
    me_zl = lax.axis_index("zl")
    block_b = jnp.zeros((n_zl, n_y) + spread_b.shape, spread_b.dtype)
    block_b = ring_into(block_b, me_zl, spread_b, "y")
    block_b = ring_into(block_b, (me_zl + 1) % n_zl, other_b, "y")
    block_a = block_a.reshape(n_core, n_x, n_zh, n_zl, n_y, local_aux, nocc, rows_a)
    block_b = block_b.reshape(n_zl, n_y, n_core, n_x, n_zh, local_aux, nocc, cols_b)
    gram = jnp.einsum(
        "cxhzypia,zycxhpjb->iajb",
        block_a,
        block_b,
        preferred_element_type=jnp.float32,
    )
    first = pair_list[:, 0]
    second = pair_list[:, 1]
    kernel = gram[first, :, second, :]
    vir_a = lax.dynamic_slice_in_dim(vir_energy, row_index * rows_a, rows_a)
    vir_b = lax.dynamic_slice_in_dim(vir_energy, col_index * cols_b, cols_b)
    e_first = occ_energy[slab_orbitals[first]]
    e_second = occ_energy[slab_orbitals[second]]
    shift = state_shift[pair_state]
    denom = (
        (vir_a[None, :, None] + vir_b[None, None, :])
        - e_first[:, None, None]
        - e_second[:, None, None]
        + shift[:, None, None]
    )
    return -kernel / denom


def solution(mesh):
    n_row, n_col = mesh.devices.shape
    sub = Mesh(mesh.devices.reshape(2, n_row // 2, n_col // 4, 2, 2), ("zl", "y", "x", "zh", "core"))
    placed = (P(("zl", "y", "x", "zh", "core"), None, None), P(), P(), P(), P(), P(), P())
    return jax.shard_map(
        shards, mesh=sub, in_specs=placed, out_specs=P(None, ("zl", "y"), ("x", "zh", "core")), check_vma=False
    )
```
